512 devices in a mesh: fsdp: 128 (over z, x_lo, y), dp: 4 (over x_hi, core).
Axes of the slice: x: 4 (x_hi: 2, x_lo: 2; x = x_hi * 2 + x_lo), y: 8, z: 8, core: 2. Of those that a mesh axis runs over, the one named last changes fastest.
Arguments:
- glu_input: bfloat16 [131072, 3072], P(('fsdp', 'dp')), may hold values from -6 to 6
- frame_counts: int32 [512, 8], P(('fsdp', 'dp')), may hold values from 1 to 128, as said below
- send_rows: int32 [512, 256], P(('fsdp', 'dp')), may hold values from 0 to 256, as said below
- owner_rows: int32 [512, 160], P(('fsdp', 'dp')), may hold values from 0 to 255, as said below
- depth_kernel: float32 [5, 1536], replicated, may hold values from -2.5 to 2.5
- norm_gain: float32 [1536], replicated, may hold values from 0.25 to 1.75
- norm_bias: float32 [1536], replicated, may hold values from -3 to 3
- point_weight: bfloat16 [1536, 1536], P('fsdp'), may hold values from -0.15625 to 0.15625
- cotangent: bfloat16 [81920, 1536], P(('fsdp', 'dp')), may hold values from -6 to 6
Outputs:
- output: bfloat16 [81920, 1536], P(('fsdp', 'dp'))
- input_grad: bfloat16 [131072, 3072], P(('fsdp', 'dp'))
- kernel_grad: float32 [5, 1536], replicated
- norm_grad: float32 [2, 1536], replicated
The draws below stay inside these ranges and needn't reach their ends.
Inputs may be any that keep to these rules, and one draw needn't show every extreme that they name: `frame_counts`: A device's counts are the lengths of its 8 utterances. A device's total lies from 64 to 256, both reached at every dp index, and the totals of the devices with one dp index sum to 160 times the fsdp axis size. The longest utterance is reached at every dp index. `send_rows`: entry q of a device's list names the local slot whose activation goes to fsdp index q // 2 with the same dp index, as that owner's position q % 2 from this device; the value 256 marks an unused entry. Each live slot is named once, positions for one owner are used from the lowest up, and some device of every dp index fills all 2 positions for every owner. `owner_rows`: entry b names received position p: position p % 2 from fsdp index p // 2 of the same dp index. The 160 entries are distinct and are exactly the positions that senders use for this owner.
All inputs are finite; a program needn't handle non-finite values.
Results may differ from the reference program's by a relative error of at most 0.0085.
Values may be sent and summed in bfloat16 or wider, within the bound.
No kernel may reach another device: no remote copies, remote signals or barrier semaphores. Data moves between devices by JAX's collectives and lax.ppermute only.
A program may use at most 64 MiB of HBM per device.

```python
import math
import jax
import jax.numpy as jnp
from jax import lax

CHANNELS = 1536
MODEL = 1536
KERNEL = 5
UTTS = 8
ROWS_DEV = 256
PEER_SLOTS = 2
OWNED = 160
ROWS = 131072
OWNED_ALL = 81920
N_FSDP = 128
N_DP = 4


def group_plan(key):
    devices = N_FSDP
    peer_slots = PEER_SLOTS
    owned_count = OWNED
    slot_count = ROWS_DEV
    base_share = owned_count // devices
    extra_owners = owned_count % devices
    pair_key, gain_key, row_key, owner_key, split_key = jax.random.split(key, 5)
    pair_order = jax.random.permutation(pair_key, devices)
    gainers = pair_order[0::2]
    losers = pair_order[1::2]
    surplus = jax.random.randint(gain_key, (devices // 2,), 0, slot_count - owned_count + 1)
    surplus = surplus.at[0].set(slot_count - owned_count)
    totals = jnp.zeros((devices,), jnp.int32).at[gainers].set(owned_count + surplus).at[losers].set(owned_count - surplus)
    source = jnp.arange(devices)[:, None]
    target = jnp.arange(devices)[None, :]
    base_count = base_share + ((target - source) % devices < extra_owners).astype(jnp.int32)
    offset = (target - gainers[:, None] - extra_owners) % devices
    wide_room = peer_slots - base_share
    room_left = jnp.where(offset < devices - extra_owners, wide_room, wide_room - 1)
    before = jnp.where(offset <= devices - extra_owners, offset * wide_room, (devices - extra_owners) * wide_room + (offset - devices + extra_owners) * (wide_room - 1))
    added = jnp.clip(surplus[:, None] - before, 0, room_left)
    counts = base_count.at[gainers].add(added).at[losers].add(-added)
    position = jnp.arange(slot_count)
    owner_of = position // peer_slots
    within = position % peer_slots
    live_send = within[None, :] < counts[:, owner_of]
    send_rank = jnp.clip(jnp.cumsum(live_send.astype(jnp.int32), axis=1) - 1, 0, slot_count - 1)

    def order_rows(sort_seed, total):
        shuffled = jax.random.permutation(sort_seed, slot_count)
        sort_keys = jnp.where(shuffled < total, position, slot_count + position)
        return shuffled[jnp.argsort(sort_keys, stable=True)]
    row_order = jax.vmap(order_rows)(jax.random.split(row_key, devices), totals)
    send_list = jnp.where(live_send, jnp.take_along_axis(row_order, send_rank, axis=1), slot_count)
    live_recv = within[None, :] < counts.T[:, owner_of]

    def order_slots(sort_seed, live_flags):
        shuffled = jax.random.permutation(sort_seed, slot_count)
        sort_keys = jnp.where(live_flags[shuffled], position, slot_count + position)
        return shuffled[jnp.argsort(sort_keys, stable=True)][:owned_count]
    owner_list = jax.vmap(order_slots)(jax.random.split(owner_key, devices), live_recv)
    weights = jax.random.randint(split_key, (devices, UTTS), 1, 6)
    cum_weight = jnp.cumsum(weights, axis=1)
    bounds = totals[:, None] * cum_weight // cum_weight[:, -1:]
    lengths = bounds - jnp.concatenate([jnp.zeros((devices, 1), bounds.dtype), bounds[:, :-1]], axis=1)
    first_full = gainers[0]
    half_rows = slot_count // 2
    rest_cum = jnp.cumsum(weights[first_full, 1:])
    rest_bounds = (slot_count - half_rows) * rest_cum // rest_cum[-1]
    rest_lengths = rest_bounds - jnp.concatenate([jnp.zeros((1,), rest_bounds.dtype), rest_bounds[:-1]])
    special = jnp.concatenate([jnp.full((1,), half_rows, rest_lengths.dtype), rest_lengths])
    lengths = lengths.at[first_full].set(special.astype(lengths.dtype))
    return (lengths, send_list, owner_list)


def full_plan(key):
    group_keys = jax.random.split(jax.random.fold_in(key, 11), N_DP)
    lengths, send_list, owner_list = jax.vmap(group_plan)(group_keys)

    def flatten(table):
        return jnp.swapaxes(table, 0, 1).reshape(N_FSDP * N_DP, table.shape[-1]).astype(jnp.int32)
    return (flatten(lengths), flatten(send_list), flatten(owner_list))


def draw_frame_counts(key, part):
    return full_plan(key)[0]


def draw_send_rows(key, part):
    return full_plan(key)[1]


def draw_owner_rows(key, part):
    return full_plan(key)[2]


def block_scale(key, extent, pieces, low, top_value):
    level, own = 1.0, jax.random.fold_in(key, 6)
    for dim, parts in pieces:
        steps = jnp.exp(jax.random.uniform(jax.random.fold_in(own, dim), (parts,), jnp.float32, low / len(pieces), top_value / len(pieces)))
        level = level * jnp.repeat(steps, extent[dim] // parts).reshape([-1 if axis == dim else 1 for axis in range(len(extent))])
    return level


def gaussian(key, extent, deviation, bound, cuts=(), kind=jnp.bfloat16):
    loudness = block_scale(key, extent, cuts, -0.22, 0.18) if cuts else 1.0
    array = jax.random.normal(key, extent, jnp.float32) * deviation * loudness
    return jnp.minimum(jnp.maximum(array, -bound), bound).astype(kind)


def setup_inputs(seed: int = 0) -> dict:
    keys = jax.random.split(jax.random.key(seed), 10)
    return {
        "glu_input": gaussian(keys[0], (ROWS, 2 * CHANNELS), 1.0, 6.0, ((0, 512),)),
        "frame_counts": draw_frame_counts(jax.random.fold_in(keys[9], 71), 0),
        "send_rows": draw_send_rows(jax.random.fold_in(keys[9], 71), 0),
        "owner_rows": draw_owner_rows(jax.random.fold_in(keys[9], 71), 0),
        "depth_kernel": gaussian(keys[4], (KERNEL, CHANNELS), KERNEL ** -0.5, 2.5, (), jnp.float32),
        "norm_gain": jnp.clip(1.0 + 0.15 * jax.random.normal(keys[5], (CHANNELS,), jnp.float32), 0.25, 1.75),
        "norm_bias": gaussian(keys[6], (CHANNELS,), 0.5, 3.0, (), jnp.float32),
        "point_weight": gaussian(keys[7], (CHANNELS, MODEL), CHANNELS ** -0.5, 0.15625, ((0, 128),)),
        "cotangent": gaussian(keys[8], (OWNED_ALL, MODEL), 1.0, 6.0, ((0, 512),)),
    }


eps = 1e-05

def conv_module(glu_rows, counts, kernel, gain_vec, bias_vec):
    row_count = glu_rows.shape[0]
    chan_count = kernel.shape[1]
    half_width = kernel.shape[0] // 2
    values = glu_rows.astype(jnp.float32)
    mixed_vals = values[:, :chan_count] * jax.nn.sigmoid(values[:, chan_count:])
    utter_ends = jnp.cumsum(counts.astype(jnp.int32))
    position = jnp.arange(row_count, dtype=jnp.int32)
    segment = lax.optimization_barrier(jnp.sum((position[:, None] >= utter_ends[None, :]).astype(jnp.int32), axis=1))
    is_live = position < utter_ends[-1]
    mixed_vals = jnp.where(is_live[:, None], mixed_vals, 0.0)
    padded = jnp.pad(mixed_vals, ((half_width, half_width), (0, 0)))
    labels = jnp.pad(segment, (half_width, half_width), constant_values=-1)
    conv_out = jnp.zeros((row_count, chan_count), jnp.float32)
    for offset in range(2 * half_width + 1):
        same_utt = labels[offset:offset + row_count] == segment
        conv_out = conv_out + jnp.where(same_utt[:, None], padded[offset:offset + row_count], 0.0) * kernel[offset]
    center = lax.optimization_barrier(jnp.mean(conv_out, axis=1, keepdims=True))
    spread = lax.optimization_barrier(jnp.mean(jnp.square(conv_out - center), axis=1, keepdims=True))
    normed = (conv_out - center) * lax.rsqrt(spread + eps) * gain_vec + bias_vec
    activated = normed * jax.nn.sigmoid(normed)
    return jnp.where(is_live[:, None], activated, 0.0)

def reference(glu_input, frame_counts, send_rows, owner_rows, depth_kernel, norm_gain, norm_bias, point_weight, cotangent):
    block_count = N_FSDP * N_DP
    glu_blocks = glu_input.reshape(block_count, ROWS_DEV, 2 * CHANNELS)

    def forward_block(block_items):
        return conv_module(block_items[0], block_items[1], depth_kernel, norm_gain, norm_bias).astype(jnp.bfloat16)
    activations = lax.map(forward_block, (glu_blocks, frame_counts)).reshape(block_count * ROWS_DEV, CHANNELS)
    owner_block = jnp.arange(block_count, dtype=jnp.int32)
    fsdp_index = owner_block // N_DP
    dp_index = owner_block % N_DP
    received_at = owner_rows.astype(jnp.int32)
    source_block = received_at // PEER_SLOTS * N_DP + dp_index[:, None]
    send_entry = fsdp_index[:, None] * PEER_SLOTS + received_at % PEER_SLOTS
    local_row = send_rows[source_block, send_entry].astype(jnp.int32)
    source_row = (source_block * ROWS_DEV + local_row).reshape(-1)
    owned_rows = activations[source_row]
    output = jnp.dot(owned_rows, point_weight, preferred_element_type=jnp.float32).astype(jnp.bfloat16)
    back_rows = jnp.dot(cotangent, point_weight.T, preferred_element_type=jnp.float32).astype(jnp.bfloat16)
    returned = jnp.zeros((block_count * ROWS_DEV, CHANNELS), jnp.bfloat16).at[source_row].set(back_rows)

    def backward_block(block_items):
        glu_block, counts, grad_block = block_items

        def local_pass(glu_rows, kernel, gain_vec, bias_vec):
            return conv_module(glu_rows, counts, kernel, gain_vec, bias_vec)
        unused, pullback = jax.vjp(local_pass, glu_block, depth_kernel, norm_gain, norm_bias)
        return pullback(grad_block.astype(jnp.float32))
    grad_parts = lax.map(backward_block, (glu_blocks, frame_counts, returned.reshape(block_count, ROWS_DEV, CHANNELS)))
    input_grad = grad_parts[0].reshape(block_count * ROWS_DEV, 2 * CHANNELS)
    grad_scale = 1.0 / math.sqrt(OWNED_ALL)
    kernel_grad = lax.optimization_barrier(jnp.sum(grad_parts[1], axis=0)) * grad_scale
    norm_grad = jnp.stack([lax.optimization_barrier(jnp.sum(grad_parts[2], axis=0)), lax.optimization_barrier(jnp.sum(grad_parts[3], axis=0))]) * grad_scale
    return (output, input_grad, kernel_grad, norm_grad)
```

```python
import math

import jax
import jax.numpy as jnp
from jax import lax
from jax.sharding import Mesh, PartitionSpec as P

eps = 1e-05

FSDP = ("z", "xl", "y")
DP = ("xh", "c")
ALL = FSDP + DP


def gather_weight(w):
    w = lax.all_gather(w, "y", axis=0, tiled=True)
    w = lax.all_gather(w, "xl", axis=0, tiled=True)
    return lax.all_gather(w, "z", axis=0, tiled=True)


def sum_all(tree):
    for axis in ("c", "xh", "xl", "y", "z"):
        tree = lax.psum(tree, axis)
    return tree


def conv_module(glu_rows, counts, kernel, gain_vec, bias_vec):
    row_count = glu_rows.shape[0]
    chan_count = kernel.shape[1]
    half_width = kernel.shape[0] // 2
    values = glu_rows.astype(jnp.float32)
    mixed_vals = values[:, :chan_count] * jax.nn.sigmoid(values[:, chan_count:])
    utter_ends = jnp.cumsum(counts)
    position = jnp.arange(row_count, dtype=jnp.int32)
    segment = jnp.sum((position[:, None] >= utter_ends[None, :]).astype(jnp.int32), axis=1)
    is_live = position < utter_ends[-1]
    mixed_vals = jnp.where(is_live[:, None], mixed_vals, 0.0)
    padded = jnp.pad(mixed_vals, ((half_width, half_width), (0, 0)))
    labels = jnp.pad(segment, (half_width, half_width), constant_values=-1)
    conv_out = jnp.zeros((row_count, chan_count), jnp.float32)
    for offset in range(2 * half_width + 1):
        same_utt = labels[offset : offset + row_count] == segment
        conv_out = (
            conv_out
            + jnp.where(same_utt[:, None], padded[offset : offset + row_count], 0.0)
            * kernel[offset]
        )
    center = jnp.mean(conv_out, axis=1, keepdims=True)
    spread = jnp.mean(jnp.square(conv_out - center), axis=1, keepdims=True)
    normed = (conv_out - center) * lax.rsqrt(spread + eps) * gain_vec + bias_vec
    activated = normed * jax.nn.sigmoid(normed)
    return jnp.where(is_live[:, None], activated, 0.0)


def per_device(
    glu_input,
    frame_counts,
    send_rows,
    owner_rows,
    depth_kernel,
    norm_gain,
    norm_bias,
    point_weight,
    cotangent,
):
    counts = frame_counts[0]
    send_slot = send_rows[0]
    owner_slot = owner_rows[0]
    row_count = glu_input.shape[0]
    out_count = point_weight.shape[1]

    def local_pass(glu_rows, kernel, gain_vec, bias_vec):
        return conv_module(glu_rows, counts, kernel, gain_vec, bias_vec)

    activated, pullback = jax.vjp(local_pass, glu_input, depth_kernel, norm_gain, norm_bias)
    activations = activated.astype(jnp.bfloat16)
    full_weight = gather_weight(point_weight)
    produced = jnp.dot(
        activations,
        full_weight,
        preferred_element_type=jnp.float32,
    ).astype(jnp.bfloat16)
    outgoing = jnp.concatenate([produced, jnp.zeros((1, out_count), jnp.bfloat16)], axis=0)[
        send_slot
    ]
    arrived = lax.all_to_all(outgoing, FSDP, split_axis=0, concat_axis=0, tiled=True)
    output = arrived[owner_slot]
    parked = jnp.zeros((row_count, out_count), jnp.bfloat16).at[owner_slot].set(cotangent)
    returned = lax.all_to_all(parked, FSDP, split_axis=0, concat_axis=0, tiled=True)
    home_rows = (
        jnp.zeros((row_count + 1, out_count), jnp.bfloat16).at[send_slot].set(returned)[:row_count]
    )
    grad_acts = lax.dot_general(
        home_rows,
        full_weight,
        (((1,), (1,)), ((), ())),
        preferred_element_type=jnp.float32,
    ).astype(jnp.bfloat16)
    input_grad, kernel_part, gain_part, bias_part = pullback(grad_acts.astype(jnp.float32))
    totals = sum_all((kernel_part, jnp.stack([gain_part, bias_part])))
    frame_total = owner_slot.shape[0] * lax.axis_size(ALL)
    grad_scale = 1.0 / math.sqrt(frame_total)
    return (output, input_grad, totals[0] * grad_scale, totals[1] * grad_scale)


def split_mesh(mesh):
    n_fsdp, n_dp = mesh.shape["fsdp"], mesh.shape["dp"]
    shape = (n_fsdp // 16, 2, 8, n_dp // 2, 2)
    return Mesh(mesh.devices.reshape(shape), FSDP + DP)


def solution(mesh):
    in_specs = (
        P(ALL, None),
        P(ALL, None),
        P(ALL, None),
        P(ALL, None),
        P(),
        P(),
        P(),
        P(FSDP, None),
        P(ALL, None),
    )
    out_specs = (P(ALL, None), P(ALL, None), P(), P())
    return jax.shard_map(
        per_device, mesh=split_mesh(mesh), in_specs=in_specs, out_specs=out_specs, check_vma=False
    )
```

```python
import math

import jax
import jax.numpy as jnp
from jax import lax
from jax.sharding import Mesh, PartitionSpec as P

eps = 1e-05

FSDP = ("z", "xl", "y")
DP = ("xh", "c")
ALL = FSDP + DP


def gather_weight(w):
    n_y = lax.axis_size("y")
    copies = jnp.broadcast_to(w[None], (n_y,) + w.shape).reshape(n_y * w.shape[0], w.shape[1])
    w = lax.all_to_all(copies, "y", 0, 0, tiled=True)
    w = lax.all_gather(w, "xl", axis=0, tiled=True)
    return lax.all_gather(w, "z", axis=0, tiled=True)


def sum_all(parts):
    n_f = lax.axis_size(FSDP)
    flat = parts.reshape(n_f, -1)
    mine = lax.all_to_all(flat, FSDP, 0, 0, tiled=True).sum(0, keepdims=True)
    mine = lax.psum(lax.psum(mine, "c"), "xh")
    whole = lax.all_to_all(jnp.broadcast_to(mine, flat.shape), FSDP, 0, 0, tiled=True)
    return whole.reshape(parts.shape)


def conv_module(glu_rows, counts, kernel, gain_vec, bias_vec):
    row_count = glu_rows.shape[0]
    chan_count = kernel.shape[1]
    half_width = kernel.shape[0] // 2
    values = glu_rows.astype(jnp.float32)
    mixed_vals = values[:, :chan_count] * jax.nn.sigmoid(values[:, chan_count:])
    utter_ends = jnp.cumsum(counts)
    position = jnp.arange(row_count, dtype=jnp.int32)
    segment = jnp.sum((position[:, None] >= utter_ends[None, :]).astype(jnp.int32), axis=1)
    is_live = position < utter_ends[-1]
    mixed_vals = jnp.where(is_live[:, None], mixed_vals, 0.0)
    padded = jnp.pad(mixed_vals, ((half_width, half_width), (0, 0)))
    labels = jnp.pad(segment, (half_width, half_width), constant_values=-1)
    conv_out = jnp.zeros((row_count, chan_count), jnp.float32)
    for offset in range(2 * half_width + 1):
        same_utt = labels[offset : offset + row_count] == segment
        conv_out = (
            conv_out
            + jnp.where(same_utt[:, None], padded[offset : offset + row_count], 0.0)
            * kernel[offset]
        )
    center = jnp.mean(conv_out, axis=1, keepdims=True)
    spread = jnp.mean(jnp.square(conv_out - center), axis=1, keepdims=True)
    normed = (conv_out - center) * lax.rsqrt(spread + eps) * gain_vec + bias_vec
    activated = normed * jax.nn.sigmoid(normed)
    return jnp.where(is_live[:, None], activated, 0.0)


def per_device(
    glu_input,
    frame_counts,
    send_rows,
    owner_rows,
    depth_kernel,
    norm_gain,
    norm_bias,
    point_weight,
    cotangent,
):
    counts = frame_counts[0]
    send_slot = send_rows[0]
    owner_slot = owner_rows[0]
    row_count = glu_input.shape[0]
    out_count = point_weight.shape[1]

    def local_pass(glu_rows, kernel, gain_vec, bias_vec):
        return conv_module(glu_rows, counts, kernel, gain_vec, bias_vec)

    activated, pullback = jax.vjp(local_pass, glu_input, depth_kernel, norm_gain, norm_bias)
    activations = activated.astype(jnp.bfloat16)
    outgoing = jnp.concatenate([activations, jnp.zeros((1, out_count), jnp.bfloat16)], axis=0)[
        send_slot
    ]
    parked = jnp.zeros((row_count, out_count), jnp.bfloat16).at[owner_slot].set(cotangent)
    moved = lax.all_to_all(
        jnp.concatenate([outgoing, parked], axis=1), FSDP, split_axis=0, concat_axis=0, tiled=True
    )
    arrived, returned = moved[:, :out_count], moved[:, out_count:]
    full_weight = gather_weight(point_weight)
    output = jnp.dot(
        arrived[owner_slot], full_weight, preferred_element_type=jnp.float32
    ).astype(jnp.bfloat16)
    home_rows = (
        jnp.zeros((row_count + 1, out_count), jnp.bfloat16).at[send_slot].set(returned)[:row_count]
    )
    grad_acts = lax.dot_general(
        home_rows,
        full_weight,
        (((1,), (1,)), ((), ())),
        preferred_element_type=jnp.float32,
    ).astype(jnp.bfloat16)
    input_grad, kernel_part, gain_part, bias_part = pullback(grad_acts.astype(jnp.float32))
    totals = sum_all(jnp.concatenate([kernel_part, gain_part[None], bias_part[None]], axis=0))
    totals = (totals[: kernel_part.shape[0]], totals[kernel_part.shape[0] :])
    frame_total = owner_slot.shape[0] * lax.axis_size(ALL)
    grad_scale = 1.0 / math.sqrt(frame_total)
    return (output, input_grad, totals[0] * grad_scale, totals[1] * grad_scale)


def split_mesh(mesh):
    n_fsdp, n_dp = mesh.shape["fsdp"], mesh.shape["dp"]
    shape = (n_fsdp // 16, 2, 8, n_dp // 2, 2)
    return Mesh(mesh.devices.reshape(shape), FSDP + DP)


def solution(mesh):
    in_specs = (
        P(ALL, None),
        P(ALL, None),
        P(ALL, None),
        P(ALL, None),
        P(),
        P(),
        P(),
        P(FSDP, None),
        P(ALL, None),
    )
    out_specs = (P(ALL, None), P(ALL, None), P(), P())
    return jax.shard_map(
        per_device, mesh=split_mesh(mesh), in_specs=in_specs, out_specs=out_specs, check_vma=False
    )
```

```python
import math

import jax
import jax.numpy as jnp
from jax import lax
from jax.sharding import Mesh, PartitionSpec as P

eps = 1e-05

FSDP = ("z", "xl", "y")
DP = ("xh", "c")
ALL = FSDP + DP


def gather_over_fsdp(w):
    n_y = lax.axis_size("y")
    copies = jnp.broadcast_to(w[None], (n_y,) + w.shape).reshape(n_y * w.shape[0], w.shape[1])
    w = lax.all_to_all(copies, "y", 0, 0, tiled=True)
    w = lax.all_gather(w, "xl", axis=0, tiled=True)
    return lax.all_gather(w, "z", axis=0, tiled=True)


def gather_weight(w):
    width = w.shape[1] // 2
    core = lax.axis_index("c")
    mine = gather_over_fsdp(lax.dynamic_slice_in_dim(w, core * width, width, axis=1))
    other = lax.ppermute(mine, "c", [(0, 1), (1, 0)])
    return jnp.where(
        core == 0, jnp.concatenate([mine, other], axis=1), jnp.concatenate([other, mine], axis=1)
    )


def sum_all(parts):
    n_f = lax.axis_size(FSDP)
    flat = parts.reshape(n_f, -1)
    mine = lax.all_to_all(flat, FSDP, 0, 0, tiled=True).sum(0, keepdims=True)
    mine = lax.psum(lax.psum(mine, "c"), "xh")
    whole = lax.all_to_all(jnp.broadcast_to(mine, flat.shape), FSDP, 0, 0, tiled=True)
    return whole.reshape(parts.shape)


def conv_module(glu_rows, counts, kernel, gain_vec, bias_vec):
    row_count = glu_rows.shape[0]
    chan_count = kernel.shape[1]
    half_width = kernel.shape[0] // 2
    values = glu_rows.astype(jnp.float32)
    mixed_vals = values[:, :chan_count] * jax.nn.sigmoid(values[:, chan_count:])
    utter_ends = jnp.cumsum(counts)
    position = jnp.arange(row_count, dtype=jnp.int32)
    segment = jnp.sum((position[:, None] >= utter_ends[None, :]).astype(jnp.int32), axis=1)
    is_live = position < utter_ends[-1]
    mixed_vals = jnp.where(is_live[:, None], mixed_vals, 0.0)
    padded = jnp.pad(mixed_vals, ((half_width, half_width), (0, 0)))
    labels = jnp.pad(segment, (half_width, half_width), constant_values=-1)
    conv_out = jnp.zeros((row_count, chan_count), jnp.float32)
    for offset in range(2 * half_width + 1):
        same_utt = labels[offset : offset + row_count] == segment
        conv_out = (
            conv_out
            + jnp.where(same_utt[:, None], padded[offset : offset + row_count], 0.0)
            * kernel[offset]
        )
    center = jnp.mean(conv_out, axis=1, keepdims=True)
    spread = jnp.mean(jnp.square(conv_out - center), axis=1, keepdims=True)
    normed = (conv_out - center) * lax.rsqrt(spread + eps) * gain_vec + bias_vec
    activated = normed * jax.nn.sigmoid(normed)
    return jnp.where(is_live[:, None], activated, 0.0)


def per_device(
    glu_input,
    frame_counts,
    send_rows,
    owner_rows,
    depth_kernel,
    norm_gain,
    norm_bias,
    point_weight,
    cotangent,
):
    counts = frame_counts[0]
    send_slot = send_rows[0]
    owner_slot = owner_rows[0]
    row_count = glu_input.shape[0]
    out_count = point_weight.shape[1]

    def local_pass(glu_rows, kernel, gain_vec, bias_vec):
        return conv_module(glu_rows, counts, kernel, gain_vec, bias_vec)

    activated, pullback = jax.vjp(local_pass, glu_input, depth_kernel, norm_gain, norm_bias)
    activations = activated.astype(jnp.bfloat16)
    outgoing = jnp.concatenate([activations, jnp.zeros((1, out_count), jnp.bfloat16)], axis=0)[
        send_slot
    ]
    parked = jnp.zeros((row_count, out_count), jnp.bfloat16).at[owner_slot].set(cotangent)
    moved = lax.all_to_all(
        jnp.concatenate([outgoing, parked], axis=1), FSDP, split_axis=0, concat_axis=0, tiled=True
    )
    arrived, returned = moved[:, :out_count], moved[:, out_count:]
    full_weight = gather_weight(point_weight)
    output = jnp.dot(
        arrived[owner_slot], full_weight, preferred_element_type=jnp.float32
    ).astype(jnp.bfloat16)
    home_rows = (
        jnp.zeros((row_count + 1, out_count), jnp.bfloat16).at[send_slot].set(returned)[:row_count]
    )
    grad_acts = lax.dot_general(
        home_rows,
        full_weight,
        (((1,), (1,)), ((), ())),
        preferred_element_type=jnp.float32,
    ).astype(jnp.bfloat16)
    input_grad, kernel_part, gain_part, bias_part = pullback(grad_acts.astype(jnp.float32))
    totals = sum_all(jnp.concatenate([kernel_part, gain_part[None], bias_part[None]], axis=0))
    totals = (totals[: kernel_part.shape[0]], totals[kernel_part.shape[0] :])
    frame_total = owner_slot.shape[0] * lax.axis_size(ALL)
    grad_scale = 1.0 / math.sqrt(frame_total)
    return (output, input_grad, totals[0] * grad_scale, totals[1] * grad_scale)


def split_mesh(mesh):
    n_fsdp, n_dp = mesh.shape["fsdp"], mesh.shape["dp"]
    shape = (n_fsdp // 16, 2, 8, n_dp // 2, 2)
    return Mesh(mesh.devices.reshape(shape), FSDP + DP)


def solution(mesh):
    in_specs = (
        P(ALL, None),
        P(ALL, None),
        P(ALL, None),
        P(ALL, None),
        P(),
        P(),
        P(),
        P(FSDP, None),
        P(ALL, None),
    )
    out_specs = (P(ALL, None), P(ALL, None), P(), P())
    return jax.shard_map(
        per_device, mesh=split_mesh(mesh), in_specs=in_specs, out_specs=out_specs, check_vma=False
    )
```

```python
import math

import jax
import jax.numpy as jnp
from jax import lax
from jax.sharding import Mesh, PartitionSpec as P

eps = 1e-05

FSDP = ("z", "xl", "y")
DP = ("xh", "c")
ALL = FSDP + DP


def gather_over_fsdp(w):
    n_y = lax.axis_size("y")
    copies = jnp.broadcast_to(w[None], (n_y,) + w.shape).reshape(n_y * w.shape[0], w.shape[1])
    w = lax.all_to_all(copies, "y", 0, 0, tiled=True)
    w = lax.all_gather(w, "xl", axis=0, tiled=True)
    return lax.all_gather(w, "z", axis=0, tiled=True)


def swap_join(mine, axis_name):
    other = lax.ppermute(mine, axis_name, [(0, 1), (1, 0)])
    first = lax.axis_index(axis_name) == 0
    return jnp.where(
        first, jnp.concatenate([mine, other], axis=1), jnp.concatenate([other, mine], axis=1)
    )


def gather_weight(w):
    width = w.shape[1] // 4
    quarter = lax.axis_index("c") * 2 + lax.axis_index("xh")
    mine = gather_over_fsdp(lax.dynamic_slice_in_dim(w, quarter * width, width, axis=1))
    return swap_join(swap_join(mine, "xh"), "c")


def sum_all(parts):
    n_f = lax.axis_size(FSDP)
    flat = parts.reshape(n_f, -1)
    mine = lax.all_to_all(flat, FSDP, 0, 0, tiled=True).sum(0, keepdims=True)
    mine = lax.psum(lax.psum(mine, "c"), "xh")
    whole = lax.all_to_all(jnp.broadcast_to(mine, flat.shape), FSDP, 0, 0, tiled=True)
    return whole.reshape(parts.shape)


def conv_module(glu_rows, counts, kernel, gain_vec, bias_vec):
    row_count = glu_rows.shape[0]
    chan_count = kernel.shape[1]
    half_width = kernel.shape[0] // 2
    values = glu_rows.astype(jnp.float32)
    mixed_vals = values[:, :chan_count] * jax.nn.sigmoid(values[:, chan_count:])
    utter_ends = jnp.cumsum(counts)
    position = jnp.arange(row_count, dtype=jnp.int32)
    segment = jnp.sum((position[:, None] >= utter_ends[None, :]).astype(jnp.int32), axis=1)
    is_live = position < utter_ends[-1]
    mixed_vals = jnp.where(is_live[:, None], mixed_vals, 0.0)
    padded = jnp.pad(mixed_vals, ((half_width, half_width), (0, 0)))
    labels = jnp.pad(segment, (half_width, half_width), constant_values=-1)
    conv_out = jnp.zeros((row_count, chan_count), jnp.float32)
    for offset in range(2 * half_width + 1):
        same_utt = labels[offset : offset + row_count] == segment
        conv_out = (
            conv_out
            + jnp.where(same_utt[:, None], padded[offset : offset + row_count], 0.0)
            * kernel[offset]
        )
    center = jnp.mean(conv_out, axis=1, keepdims=True)
    spread = jnp.mean(jnp.square(conv_out - center), axis=1, keepdims=True)
    normed = (conv_out - center) * lax.rsqrt(spread + eps) * gain_vec + bias_vec
    activated = normed * jax.nn.sigmoid(normed)
    return jnp.where(is_live[:, None], activated, 0.0)


def per_device(
    glu_input,
    frame_counts,
    send_rows,
    owner_rows,
    depth_kernel,
    norm_gain,
    norm_bias,
    point_weight,
    cotangent,
):
    counts = frame_counts[0]
    send_slot = send_rows[0]
    owner_slot = owner_rows[0]
    row_count = glu_input.shape[0]
    out_count = point_weight.shape[1]

    def local_pass(glu_rows, kernel, gain_vec, bias_vec):
        return conv_module(glu_rows, counts, kernel, gain_vec, bias_vec)

    activated, pullback = jax.vjp(local_pass, glu_input, depth_kernel, norm_gain, norm_bias)
    activations = activated.astype(jnp.bfloat16)
    outgoing = jnp.concatenate([activations, jnp.zeros((1, out_count), jnp.bfloat16)], axis=0)[
        send_slot
    ]
    parked = jnp.zeros((row_count, out_count), jnp.bfloat16).at[owner_slot].set(cotangent)
    moved = lax.all_to_all(
        jnp.concatenate([outgoing, parked], axis=1), FSDP, split_axis=0, concat_axis=0, tiled=True
    )
    arrived, returned = moved[:, :out_count], moved[:, out_count:]
    full_weight = gather_weight(point_weight)
    output = jnp.dot(
        arrived[owner_slot], full_weight, preferred_element_type=jnp.float32
    ).astype(jnp.bfloat16)
    home_rows = (
        jnp.zeros((row_count + 1, out_count), jnp.bfloat16).at[send_slot].set(returned)[:row_count]
    )
    grad_acts = lax.dot_general(
        home_rows,
        full_weight,
        (((1,), (1,)), ((), ())),
        preferred_element_type=jnp.float32,
    ).astype(jnp.bfloat16)
    input_grad, kernel_part, gain_part, bias_part = pullback(grad_acts.astype(jnp.float32))
    totals = sum_all(jnp.concatenate([kernel_part, gain_part[None], bias_part[None]], axis=0))
    totals = (totals[: kernel_part.shape[0]], totals[kernel_part.shape[0] :])
    frame_total = owner_slot.shape[0] * lax.axis_size(ALL)
    grad_scale = 1.0 / math.sqrt(frame_total)
    return (output, input_grad, totals[0] * grad_scale, totals[1] * grad_scale)


def split_mesh(mesh):
    n_fsdp, n_dp = mesh.shape["fsdp"], mesh.shape["dp"]
    shape = (n_fsdp // 16, 2, 8, n_dp // 2, 2)
    return Mesh(mesh.devices.reshape(shape), FSDP + DP)


def solution(mesh):
    in_specs = (
        P(ALL, None),
        P(ALL, None),
        P(ALL, None),
        P(ALL, None),
        P(),
        P(),
        P(),
        P(FSDP, None),
        P(ALL, None),
    )
    out_specs = (P(ALL, None), P(ALL, None), P(), P())
    return jax.shard_map(
        per_device, mesh=split_mesh(mesh), in_specs=in_specs, out_specs=out_specs, check_vma=False
    )
```

```python
import math

import jax
import jax.numpy as jnp
from jax import lax
from jax.sharding import Mesh, PartitionSpec as P

eps = 1e-05

FSDP = ("z", "xl", "y")
DP = ("xh", "c")
ALL = FSDP + DP


def gather_over_fsdp(w):
    n_y = lax.axis_size("y")
    copies = jnp.broadcast_to(w[None], (n_y,) + w.shape).reshape(n_y * w.shape[0], w.shape[1])
    w = lax.all_to_all(copies, "y", 0, 0, tiled=True)
    w = lax.all_gather(w, "xl", axis=0, tiled=True)
    return lax.all_gather(w, "z", axis=0, tiled=True)


def swap_join(mine, axis_name):
    other = lax.ppermute(mine, axis_name, [(0, 1), (1, 0)])
    first = lax.axis_index(axis_name) == 0
    return jnp.where(
        first, jnp.concatenate([mine, other], axis=1), jnp.concatenate([other, mine], axis=1)
    )


def fetch_quarter(w):
    width = w.shape[1] // 4
    quarter = lax.axis_index("c") * 2 + lax.axis_index("xh")
    return gather_over_fsdp(lax.dynamic_slice_in_dim(w, quarter * width, width, axis=1))


def join_quarters(mine):
    return swap_join(swap_join(mine, "xh"), "c")


def sum_all(parts):
    n_f = lax.axis_size(FSDP)
    flat = parts.reshape(n_f, -1)
    mine = lax.all_to_all(flat, FSDP, 0, 0, tiled=True).sum(0, keepdims=True)
    mine = lax.psum(lax.psum(mine, "c"), "xh")
    whole = lax.all_to_all(jnp.broadcast_to(mine, flat.shape), FSDP, 0, 0, tiled=True)
    return whole.reshape(parts.shape)


def conv_module(glu_rows, counts, kernel, gain_vec, bias_vec):
    row_count = glu_rows.shape[0]
    chan_count = kernel.shape[1]
    half_width = kernel.shape[0] // 2
    values = glu_rows.astype(jnp.float32)
    mixed_vals = values[:, :chan_count] * jax.nn.sigmoid(values[:, chan_count:])
    utter_ends = jnp.cumsum(counts)
    position = jnp.arange(row_count, dtype=jnp.int32)
    segment = jnp.sum((position[:, None] >= utter_ends[None, :]).astype(jnp.int32), axis=1)
    is_live = position < utter_ends[-1]
    mixed_vals = jnp.where(is_live[:, None], mixed_vals, 0.0)
    padded = jnp.pad(mixed_vals, ((half_width, half_width), (0, 0)))
    labels = jnp.pad(segment, (half_width, half_width), constant_values=-1)
    conv_out = jnp.zeros((row_count, chan_count), jnp.float32)
    for offset in range(2 * half_width + 1):
        same_utt = labels[offset : offset + row_count] == segment
        conv_out = (
            conv_out
            + jnp.where(same_utt[:, None], padded[offset : offset + row_count], 0.0)
            * kernel[offset]
        )
    center = jnp.mean(conv_out, axis=1, keepdims=True)
    spread = jnp.mean(jnp.square(conv_out - center), axis=1, keepdims=True)
    normed = (conv_out - center) * lax.rsqrt(spread + eps) * gain_vec + bias_vec
    activated = normed * jax.nn.sigmoid(normed)
    return jnp.where(is_live[:, None], activated, 0.0)


def per_device(
    glu_input,
    frame_counts,
    send_rows,
    owner_rows,
    depth_kernel,
    norm_gain,
    norm_bias,
    point_weight,
    cotangent,
):
    counts = frame_counts[0]
    send_slot = send_rows[0]
    owner_slot = owner_rows[0]
    row_count = glu_input.shape[0]
    out_count = point_weight.shape[1]

    def local_pass(glu_rows, kernel, gain_vec, bias_vec):
        return conv_module(glu_rows, counts, kernel, gain_vec, bias_vec)

    activated, pullback = jax.vjp(local_pass, glu_input, depth_kernel, norm_gain, norm_bias)
    activations = activated.astype(jnp.bfloat16)
    outgoing = jnp.concatenate([activations, jnp.zeros((1, out_count), jnp.bfloat16)], axis=0)[
        send_slot
    ]
    parked = jnp.zeros((row_count, out_count), jnp.bfloat16).at[owner_slot].set(cotangent)
    moved = lax.all_to_all(
        jnp.concatenate([outgoing, parked], axis=1), FSDP, split_axis=0, concat_axis=0, tiled=True
    )
    quarter_weight, moved = lax.optimization_barrier((fetch_quarter(point_weight), moved))
    arrived, returned = moved[:, :out_count], moved[:, out_count:]
    full_weight = join_quarters(quarter_weight)
    output = jnp.dot(
        arrived[owner_slot], full_weight, preferred_element_type=jnp.float32
    ).astype(jnp.bfloat16)
    home_rows = (
        jnp.zeros((row_count + 1, out_count), jnp.bfloat16).at[send_slot].set(returned)[:row_count]
    )
    grad_acts = lax.dot_general(
        home_rows,
        full_weight,
        (((1,), (1,)), ((), ())),
        preferred_element_type=jnp.float32,
    ).astype(jnp.bfloat16)
    input_grad, kernel_part, gain_part, bias_part = pullback(grad_acts.astype(jnp.float32))
    totals = sum_all(jnp.concatenate([kernel_part, gain_part[None], bias_part[None]], axis=0))
    totals = (totals[: kernel_part.shape[0]], totals[kernel_part.shape[0] :])
    frame_total = owner_slot.shape[0] * lax.axis_size(ALL)
    grad_scale = 1.0 / math.sqrt(frame_total)
    return (output, input_grad, totals[0] * grad_scale, totals[1] * grad_scale)


def split_mesh(mesh):
    n_fsdp, n_dp = mesh.shape["fsdp"], mesh.shape["dp"]
    shape = (n_fsdp // 16, 2, 8, n_dp // 2, 2)
    return Mesh(mesh.devices.reshape(shape), FSDP + DP)


def solution(mesh):
    in_specs = (
        P(ALL, None),
        P(ALL, None),
        P(ALL, None),
        P(ALL, None),
        P(),
        P(),
        P(),
        P(FSDP, None),
        P(ALL, None),
    )
    out_specs = (P(ALL, None), P(ALL, None), P(), P())
    return jax.shard_map(
        per_device, mesh=split_mesh(mesh), in_specs=in_specs, out_specs=out_specs, check_vma=False
    )
```

```python
import math

import jax
import jax.numpy as jnp
from jax import lax
from jax.sharding import Mesh, PartitionSpec as P

eps = 1e-05

FSDP = ("z", "xl", "y")
DP = ("xh", "c")
ALL = FSDP + DP


def gather_over_fsdp(w):
    n_y = lax.axis_size("y")
    copies = jnp.broadcast_to(w[None], (n_y,) + w.shape).reshape(n_y * w.shape[0], w.shape[1])
    w = lax.all_to_all(copies, "y", 0, 0, tiled=True)
    w = lax.all_gather(w, "xl", axis=0, tiled=True)
    return lax.all_gather(w, "z", axis=0, tiled=True)


def gather_weight(w):
    width = w.shape[1] // 2
    core = lax.axis_index("c")
    mine = gather_over_fsdp(lax.dynamic_slice_in_dim(w, core * width, width, axis=1))
    other = lax.ppermute(mine, "c", [(0, 1), (1, 0)])
    return jnp.where(
        core == 0, jnp.concatenate([mine, other], axis=1), jnp.concatenate([other, mine], axis=1)
    )


def sum_all(parts):
    n_all = lax.axis_size(ALL)
    flat = parts.reshape(n_all, -1)
    mine = lax.all_to_all(flat, ALL, 0, 0, tiled=True).sum(0, keepdims=True)
    whole = lax.all_to_all(jnp.broadcast_to(mine, flat.shape), ALL, 0, 0, tiled=True)
    return whole.reshape(parts.shape)


def conv_module(glu_rows, counts, kernel, gain_vec, bias_vec):
    row_count = glu_rows.shape[0]
    chan_count = kernel.shape[1]
    half_width = kernel.shape[0] // 2
    values = glu_rows.astype(jnp.float32)
    mixed_vals = values[:, :chan_count] * jax.nn.sigmoid(values[:, chan_count:])
    utter_ends = jnp.cumsum(counts)
    position = jnp.arange(row_count, dtype=jnp.int32)
    segment = jnp.sum((position[:, None] >= utter_ends[None, :]).astype(jnp.int32), axis=1)
    is_live = position < utter_ends[-1]
    mixed_vals = jnp.where(is_live[:, None], mixed_vals, 0.0)
    padded = jnp.pad(mixed_vals, ((half_width, half_width), (0, 0)))
    labels = jnp.pad(segment, (half_width, half_width), constant_values=-1)
    conv_out = jnp.zeros((row_count, chan_count), jnp.float32)
    for offset in range(2 * half_width + 1):
        same_utt = labels[offset : offset + row_count] == segment
        conv_out = (
            conv_out
            + jnp.where(same_utt[:, None], padded[offset : offset + row_count], 0.0)
            * kernel[offset]
        )
    center = jnp.mean(conv_out, axis=1, keepdims=True)
    spread = jnp.mean(jnp.square(conv_out - center), axis=1, keepdims=True)
    normed = (conv_out - center) * lax.rsqrt(spread + eps) * gain_vec + bias_vec
    activated = normed * jax.nn.sigmoid(normed)
    return jnp.where(is_live[:, None], activated, 0.0)


def per_device(
    glu_input,
    frame_counts,
    send_rows,
    owner_rows,
    depth_kernel,
    norm_gain,
    norm_bias,
    point_weight,
    cotangent,
):
    counts = frame_counts[0]
    send_slot = send_rows[0]
    owner_slot = owner_rows[0]
    row_count = glu_input.shape[0]
    out_count = point_weight.shape[1]

    def local_pass(glu_rows, kernel, gain_vec, bias_vec):
        return conv_module(glu_rows, counts, kernel, gain_vec, bias_vec)

    activated, pullback = jax.vjp(local_pass, glu_input, depth_kernel, norm_gain, norm_bias)
    activations = activated.astype(jnp.bfloat16)
    outgoing = jnp.concatenate([activations, jnp.zeros((1, out_count), jnp.bfloat16)], axis=0)[
        send_slot
    ]
    parked = jnp.zeros((row_count, out_count), jnp.bfloat16).at[owner_slot].set(cotangent)
    moved = lax.all_to_all(
        jnp.concatenate([outgoing, parked], axis=1), FSDP, split_axis=0, concat_axis=0, tiled=True
    )
    arrived, returned = moved[:, :out_count], moved[:, out_count:]
    full_weight = gather_weight(point_weight)
    output = jnp.dot(
        arrived[owner_slot], full_weight, preferred_element_type=jnp.float32
    ).astype(jnp.bfloat16)
    home_rows = (
        jnp.zeros((row_count + 1, out_count), jnp.bfloat16).at[send_slot].set(returned)[:row_count]
    )
    grad_acts = lax.dot_general(
        home_rows,
        full_weight,
        (((1,), (1,)), ((), ())),
        preferred_element_type=jnp.float32,
    ).astype(jnp.bfloat16)
    input_grad, kernel_part, gain_part, bias_part = pullback(grad_acts.astype(jnp.float32))
    totals = sum_all(jnp.concatenate([kernel_part, gain_part[None], bias_part[None]], axis=0))
    totals = (totals[: kernel_part.shape[0]], totals[kernel_part.shape[0] :])
    frame_total = owner_slot.shape[0] * lax.axis_size(ALL)
    grad_scale = 1.0 / math.sqrt(frame_total)
    return (output, input_grad, totals[0] * grad_scale, totals[1] * grad_scale)


def split_mesh(mesh):
    n_fsdp, n_dp = mesh.shape["fsdp"], mesh.shape["dp"]
    shape = (n_fsdp // 16, 2, 8, n_dp // 2, 2)
    return Mesh(mesh.devices.reshape(shape), FSDP + DP)


def solution(mesh):
    in_specs = (
        P(ALL, None),
        P(ALL, None),
        P(ALL, None),
        P(ALL, None),
        P(),
        P(),
        P(),
        P(FSDP, None),
        P(ALL, None),
    )
    out_specs = (P(ALL, None), P(ALL, None), P(), P())
    return jax.shard_map(
        per_device, mesh=split_mesh(mesh), in_specs=in_specs, out_specs=out_specs, check_vma=False
    )
```

```python
import math

import jax
import jax.numpy as jnp
from jax import lax
from jax.sharding import Mesh, PartitionSpec as P

eps = 1e-05

FSDP = ("z", "xl", "y")
DP = ("xh", "c")
ALL = FSDP + DP


def gather_over_fsdp(w):
    n_y, n_z = lax.axis_size("y"), lax.axis_size("z")
    copies = jnp.broadcast_to(w[None], (n_y,) + w.shape).reshape(n_y * w.shape[0], w.shape[1])
    w = lax.all_to_all(copies, "y", 0, 0, tiled=True)
    mine = lax.all_gather(w, "z", axis=0, tiled=True).reshape(n_z, 1, -1, w.shape[1])
    return mine


def swap_rows(mine):
    other = lax.ppermute(mine, "xl", [(0, 1), (1, 0)])
    first = lax.axis_index("xl") == 0
    joined = jnp.where(
        first, jnp.concatenate([mine, other], axis=1), jnp.concatenate([other, mine], axis=1)
    )
    return joined.reshape(-1, mine.shape[-1])


def fetch_half(w):
    width = w.shape[1] // 2
    core = lax.axis_index("c")
    return gather_over_fsdp(lax.dynamic_slice_in_dim(w, core * width, width, axis=1))


def gather_weight(w):
    core = lax.axis_index("c")
    mine = swap_rows(w)
    other = lax.ppermute(mine, "c", [(0, 1), (1, 0)])
    return jnp.where(
        core == 0, jnp.concatenate([mine, other], axis=1), jnp.concatenate([other, mine], axis=1)
    )


def sum_all(parts):
    n_f = lax.axis_size(FSDP)
    flat = parts.reshape(n_f, -1)
    mine = lax.all_to_all(flat, FSDP, 0, 0, tiled=True).sum(0, keepdims=True)
    mine = lax.psum(lax.psum(mine, "c"), "xh")
    whole = lax.all_to_all(jnp.broadcast_to(mine, flat.shape), FSDP, 0, 0, tiled=True)
    return whole.reshape(parts.shape)


def conv_module(glu_rows, counts, kernel, gain_vec, bias_vec):
    row_count = glu_rows.shape[0]
    chan_count = kernel.shape[1]
    half_width = kernel.shape[0] // 2
    values = glu_rows.astype(jnp.float32)
    mixed_vals = values[:, :chan_count] * jax.nn.sigmoid(values[:, chan_count:])
    utter_ends = jnp.cumsum(counts)
    position = jnp.arange(row_count, dtype=jnp.int32)
    segment = jnp.sum((position[:, None] >= utter_ends[None, :]).astype(jnp.int32), axis=1)
    is_live = position < utter_ends[-1]
    mixed_vals = jnp.where(is_live[:, None], mixed_vals, 0.0)
    padded = jnp.pad(mixed_vals, ((half_width, half_width), (0, 0)))
    labels = jnp.pad(segment, (half_width, half_width), constant_values=-1)
    conv_out = jnp.zeros((row_count, chan_count), jnp.float32)
    for offset in range(2 * half_width + 1):
        same_utt = labels[offset : offset + row_count] == segment
        conv_out = (
            conv_out
            + jnp.where(same_utt[:, None], padded[offset : offset + row_count], 0.0)
            * kernel[offset]
        )
    center = jnp.mean(conv_out, axis=1, keepdims=True)
    spread = jnp.mean(jnp.square(conv_out - center), axis=1, keepdims=True)
    normed = (conv_out - center) * lax.rsqrt(spread + eps) * gain_vec + bias_vec
    activated = normed * jax.nn.sigmoid(normed)
    return jnp.where(is_live[:, None], activated, 0.0)


def per_device(
    glu_input,
    frame_counts,
    send_rows,
    owner_rows,
    depth_kernel,
    norm_gain,
    norm_bias,
    point_weight,
    cotangent,
):
    counts = frame_counts[0]
    send_slot = send_rows[0]
    owner_slot = owner_rows[0]
    row_count = glu_input.shape[0]
    out_count = point_weight.shape[1]

    def local_pass(glu_rows, kernel, gain_vec, bias_vec):
        return conv_module(glu_rows, counts, kernel, gain_vec, bias_vec)

    activated, pullback = jax.vjp(local_pass, glu_input, depth_kernel, norm_gain, norm_bias)
    activations = activated.astype(jnp.bfloat16)
    outgoing = jnp.concatenate([activations, jnp.zeros((1, out_count), jnp.bfloat16)], axis=0)[
        send_slot
    ]
    parked = jnp.zeros((row_count, out_count), jnp.bfloat16).at[owner_slot].set(cotangent)
    moved = lax.all_to_all(
        jnp.concatenate([outgoing, parked], axis=1), FSDP, split_axis=0, concat_axis=0, tiled=True
    )
    half_weight, moved = lax.optimization_barrier((fetch_half(point_weight), moved))
    arrived, returned = moved[:, :out_count], moved[:, out_count:]
    full_weight = gather_weight(half_weight)
    output = jnp.dot(
        arrived[owner_slot], full_weight, preferred_element_type=jnp.float32
    ).astype(jnp.bfloat16)
    home_rows = (
        jnp.zeros((row_count + 1, out_count), jnp.bfloat16).at[send_slot].set(returned)[:row_count]
    )
    grad_acts = lax.dot_general(
        home_rows,
        full_weight,
        (((1,), (1,)), ((), ())),
        preferred_element_type=jnp.float32,
    ).astype(jnp.bfloat16)
    input_grad, kernel_part, gain_part, bias_part = pullback(grad_acts.astype(jnp.float32))
    totals = sum_all(jnp.concatenate([kernel_part, gain_part[None], bias_part[None]], axis=0))
    totals = (totals[: kernel_part.shape[0]], totals[kernel_part.shape[0] :])
    frame_total = owner_slot.shape[0] * lax.axis_size(ALL)
    grad_scale = 1.0 / math.sqrt(frame_total)
    return (output, input_grad, totals[0] * grad_scale, totals[1] * grad_scale)


def split_mesh(mesh):
    n_fsdp, n_dp = mesh.shape["fsdp"], mesh.shape["dp"]
    shape = (n_fsdp // 16, 2, 8, n_dp // 2, 2)
    return Mesh(mesh.devices.reshape(shape), FSDP + DP)


def solution(mesh):
    in_specs = (
        P(ALL, None),
        P(ALL, None),
        P(ALL, None),
        P(ALL, None),
        P(),
        P(),
        P(),
        P(FSDP, None),
        P(ALL, None),
    )
    out_specs = (P(ALL, None), P(ALL, None), P(), P())
    return jax.shard_map(
        per_device, mesh=split_mesh(mesh), in_specs=in_specs, out_specs=out_specs, check_vma=False
    )
```

```python
import math

import jax
import jax.numpy as jnp
from jax import lax
from jax.sharding import Mesh, PartitionSpec as P

eps = 1e-05

FSDP = ("z", "xl", "y")
DP = ("xh", "c")
ALL = FSDP + DP


def gather_over_fsdp(w):
    n_y = lax.axis_size("y")
    copies = jnp.broadcast_to(w[None], (n_y,) + w.shape).reshape(n_y * w.shape[0], w.shape[1])
    w = lax.all_to_all(copies, "y", 0, 0, tiled=True)
    w = lax.all_gather(w, "xl", axis=0, tiled=True)
    return lax.all_gather(w, "z", axis=0, tiled=True)


def gather_weight(w):
    width = w.shape[1] // 2
    core = lax.axis_index("c")
    mine = gather_over_fsdp(lax.dynamic_slice_in_dim(w, core * width, width, axis=1))
    other = lax.ppermute(mine, "c", [(0, 1), (1, 0)])
    return jnp.where(
        core == 0, jnp.concatenate([mine, other], axis=1), jnp.concatenate([other, mine], axis=1)
    )


def sum_all(parts):
    n_f = lax.axis_size(FSDP)
    flat = parts.reshape(n_f, -1)
    mine = lax.all_to_all(flat, FSDP, 0, 0, tiled=True).sum(0, keepdims=True)
    mine = lax.psum(mine, DP)
    whole = lax.all_to_all(jnp.broadcast_to(mine, flat.shape), FSDP, 0, 0, tiled=True)
    return whole.reshape(parts.shape)


def conv_module(glu_rows, counts, kernel, gain_vec, bias_vec):
    row_count = glu_rows.shape[0]
    chan_count = kernel.shape[1]
    half_width = kernel.shape[0] // 2
    values = glu_rows.astype(jnp.float32)
    mixed_vals = values[:, :chan_count] * jax.nn.sigmoid(values[:, chan_count:])
    utter_ends = jnp.cumsum(counts)
    position = jnp.arange(row_count, dtype=jnp.int32)
    segment = jnp.sum((position[:, None] >= utter_ends[None, :]).astype(jnp.int32), axis=1)
    is_live = position < utter_ends[-1]
    mixed_vals = jnp.where(is_live[:, None], mixed_vals, 0.0)
    padded = jnp.pad(mixed_vals, ((half_width, half_width), (0, 0)))
    labels = jnp.pad(segment, (half_width, half_width), constant_values=-1)
    conv_out = jnp.zeros((row_count, chan_count), jnp.float32)
    for offset in range(2 * half_width + 1):
        same_utt = labels[offset : offset + row_count] == segment
        conv_out = (
            conv_out
            + jnp.where(same_utt[:, None], padded[offset : offset + row_count], 0.0)
            * kernel[offset]
        )
    center = jnp.mean(conv_out, axis=1, keepdims=True)
    spread = jnp.mean(jnp.square(conv_out - center), axis=1, keepdims=True)
    normed = (conv_out - center) * lax.rsqrt(spread + eps) * gain_vec + bias_vec
    activated = normed * jax.nn.sigmoid(normed)
    return jnp.where(is_live[:, None], activated, 0.0)


def per_device(
    glu_input,
    frame_counts,
    send_rows,
    owner_rows,
    depth_kernel,
    norm_gain,
    norm_bias,
    point_weight,
    cotangent,
):
    counts = frame_counts[0]
    send_slot = send_rows[0]
    owner_slot = owner_rows[0]
    row_count = glu_input.shape[0]
    out_count = point_weight.shape[1]

    def local_pass(glu_rows, kernel, gain_vec, bias_vec):
        return conv_module(glu_rows, counts, kernel, gain_vec, bias_vec)

    activated, pullback = jax.vjp(local_pass, glu_input, depth_kernel, norm_gain, norm_bias)
    activations = activated.astype(jnp.bfloat16)
    outgoing = jnp.concatenate([activations, jnp.zeros((1, out_count), jnp.bfloat16)], axis=0)[
        send_slot
    ]
    parked = jnp.zeros((row_count, out_count), jnp.bfloat16).at[owner_slot].set(cotangent)
    moved = lax.all_to_all(
        jnp.concatenate([outgoing, parked], axis=1), FSDP, split_axis=0, concat_axis=0, tiled=True
    )
    arrived, returned = moved[:, :out_count], moved[:, out_count:]
    full_weight = gather_weight(point_weight)
    output = jnp.dot(
        arrived[owner_slot], full_weight, preferred_element_type=jnp.float32
    ).astype(jnp.bfloat16)
    home_rows = (
        jnp.zeros((row_count + 1, out_count), jnp.bfloat16).at[send_slot].set(returned)[:row_count]
    )
    grad_acts = lax.dot_general(
        home_rows,
        full_weight,
        (((1,), (1,)), ((), ())),
        preferred_element_type=jnp.float32,
    ).astype(jnp.bfloat16)
    input_grad, kernel_part, gain_part, bias_part = pullback(grad_acts.astype(jnp.float32))
    totals = sum_all(jnp.concatenate([kernel_part, gain_part[None], bias_part[None]], axis=0))
    totals = (totals[: kernel_part.shape[0]], totals[kernel_part.shape[0] :])
    frame_total = owner_slot.shape[0] * lax.axis_size(ALL)
    grad_scale = 1.0 / math.sqrt(frame_total)
    return (output, input_grad, totals[0] * grad_scale, totals[1] * grad_scale)


def split_mesh(mesh):
    n_fsdp, n_dp = mesh.shape["fsdp"], mesh.shape["dp"]
    shape = (n_fsdp // 16, 2, 8, n_dp // 2, 2)
    return Mesh(mesh.devices.reshape(shape), FSDP + DP)


def solution(mesh):
    in_specs = (
        P(ALL, None),
        P(ALL, None),
        P(ALL, None),
        P(ALL, None),
        P(),
        P(),
        P(),
        P(FSDP, None),
        P(ALL, None),
    )
    out_specs = (P(ALL, None), P(ALL, None), P(), P())
    return jax.shard_map(
        per_device, mesh=split_mesh(mesh), in_specs=in_specs, out_specs=out_specs, check_vma=False
    )
```
